512 devices in a mesh: pipe: 4 (over y), expert: 32 (over z, core), tensor: 4 (over x).
Axes of the slice: x: 4, y: 4, z: 16, core: 2. Of those that a mesh axis runs over, the one named last changes fastest.
Arguments:
- tokens: bfloat16 [512, 6144], P('expert', ('pipe', 'tensor')), may hold values from -6 to 6
- expert_ids: int32 [512, 2], P('expert'), may hold values from 0 to 7, all different within a row; in each aligned block of 16 rows (0 to 15, 16 to 31, ...) at most 5 rows name the same one
- gates: float32 [512, 2], P('expert'), may hold values from 0.2 to 1
- w_gate: bfloat16 [32, 6144, 2048], P('expert', None, ('pipe', 'tensor')), may hold values from -0.078125 to 0.078125
- w_up: bfloat16 [32, 6144, 2048], P('expert', None, ('pipe', 'tensor')), may hold values from -0.078125 to 0.078125
- w_down: bfloat16 [32, 2048, 6144], P('expert', ('pipe', 'tensor')), may hold values from -0.0625 to 0.0625
- d_out: bfloat16 [512, 6144], P('expert', ('pipe', 'tensor')), may hold values from -6 to 6
Outputs:
- moe_out: bfloat16 [512, 6144], P('expert', ('pipe', 'tensor'))
- grad_tokens: bfloat16 [512, 6144], P('expert', ('pipe', 'tensor'))
- grad_gates: float32 [512, 2], P('expert')
The draws below stay inside these ranges and needn't reach their ends.
Inputs may be any that keep to these rules, and one draw needn't show every extreme that they name: `expert_ids`: each row names 2 different experts. Among the rows of one index of expert (aligned blocks of 16 rows) no expert is named more than 5 times, a bound that some block reaches.
All inputs are finite; a program needn't handle non-finite values.
Results may differ from the reference program's by a relative error of at most 0.017.
Values may be sent and summed in bfloat16 or wider, within the bound.
No kernel may reach another device: no remote copies, remote signals or barrier semaphores. Data moves between devices by JAX's collectives and lax.ppermute only.
A program may use at most 64 MiB of HBM per device.

```python
import math
import jax
import jax.numpy as jnp
import numpy as np
from jax import lax

D = 6144
HID = 8192
TOP = 2
TOK_DEV = 16
EXPERTS = 8
GROUP = 4
CAP = 5
TOKENS = 512
N_PIPE = 4
N_EXPERT = 32
N_TENSOR = 4


def block_levels(own_key, extent, cuts, low, largest):
    def one(dim, blocks):
        heights = jax.random.uniform(jax.random.fold_in(jax.random.fold_in(own_key, 6), dim), (blocks,), jnp.float32, low / len(cuts), largest / len(cuts))
        return jnp.repeat(jnp.exp(heights), extent[dim] // blocks).reshape((-1,) + (1,) * (len(extent) - dim - 1))

    loudness = one(*cuts[0])
    for cut in cuts[1:]:
        loudness = loudness * one(*cut)
    return loudness


def deal_out(own_key, own, number, rows, amount, top, bound, lean):
    sequence = jax.random.permutation(own_key, amount)
    heavy_load, usual = shares(amount, rows * top, bound, lean, True), shares(amount, rows * top, bound, lean, False)
    places = jnp.arange(amount)

    def named(sizes, offset_by):
        used = int((sizes > 0).sum())
        fixed = max(1, used // 4)
        moved = fixed + (places - fixed + offset_by * (used - fixed)) % max(1, amount - fixed)
        return jnp.zeros((amount,), jnp.int32).at[sequence[jnp.where(places < fixed, places, moved)]].set(jnp.asarray(sizes, jnp.int32))

    sizes = jnp.where(number % 4 == 0, named(heavy_load, number // 4), named(usual, number - number // 4 - 1))
    mixed = jax.random.permutation(jax.random.fold_in(own, 3), amount)
    donor, taker = mixed[0:amount // 2 * 2:2], mixed[1:amount // 2 * 2:2]
    slack = jnp.minimum(sizes[donor] - 1, bound - sizes[taker]) // 2
    slack = jnp.where((donor == sequence[0]) | (taker == sequence[0]) | (sizes[taker] == 0), 0, jnp.maximum(slack, 0))
    moved = jax.random.randint(jax.random.fold_in(own, 4), (amount // 2,), 0, 1 << 20) % (slack + 1)
    sizes = sizes.at[donor].add(-moved).at[taker].add(moved)
    items = jnp.searchsorted(jnp.cumsum(sizes), jnp.arange(rows * top), side="right").astype(jnp.int32)
    listing = items.reshape(top, rows).T
    listing = listing[jax.random.permutation(jax.random.fold_in(own, 1), rows)]
    offset_by = jax.random.randint(jax.random.fold_in(own, 2), (rows, 1), 0, top)
    return jnp.take_along_axis(listing, (jnp.arange(top)[None, :] + offset_by) % top, axis=1)


def shares(count, total, limit, slope, full):
    weights = [(1 << 20) // math.isqrt(standing ** slope) + 1 for standing in range(1, count + 1)]
    largest = limit if full else min(limit, max(-(-total // count), total * weights[0] // sum(weights)))
    least = 1 if total - largest >= count - 1 else 0
    counts, spare = [largest] + [least] * (count - 1), total - largest - least * (count - 1)
    while spare > 0:
        movable = [i for i in range(1, count) if counts[i] < largest] or [i for i in range(1, count) if counts[i] < limit]
        mass, left = sum([weights[i] for i in movable]), spare
        for i in movable:
            extra = min(limit - counts[i], max(1, left * weights[i] // mass), spare)
            counts[i] = counts[i] + extra
            spare = spare - extra
    return np.array(counts)


def gaussian(stream_key, extent, deviation, limit, cuts=(), kind=jnp.bfloat16):
    level = block_levels(stream_key, extent, cuts, -0.22, 0.18) if cuts else 1.0
    entries = jax.random.normal(stream_key, extent, jnp.float32) * deviation * level
    return jnp.minimum(jnp.maximum(entries, -limit), limit).astype(kind)


def setup_inputs(seed: int = 0) -> dict:
    keys = jax.random.split(jax.random.key(seed), 8)
    tokens = gaussian(keys[0], (TOKENS, D), 1.0, 6.0, ((0, 32), (1, 16)))
    expert_ids_keys = jax.random.split(jax.random.fold_in(keys[1], 1), TOKENS // TOK_DEV)
    expert_ids_turns = jax.random.permutation(jax.random.fold_in(keys[1], 3), TOKENS // TOK_DEV)
    expert_ids = jax.vmap(lambda own, number: deal_out(jax.random.fold_in(keys[1], 2), own, number, TOK_DEV, EXPERTS, TOP, CAP, 2))(expert_ids_keys, expert_ids_turns).reshape((TOKENS, TOP))
    gates = jnp.clip(0.2 + 0.8 * jax.random.uniform(keys[2], (TOKENS, TOP), jnp.float32) ** block_levels(keys[2], (TOKENS, TOP), ((0, 32),), -0.2, 0.2), 0.2, 1.0)
    w_gate = gaussian(keys[3], (EXPERTS * GROUP, D, HID // GROUP), D ** -0.5, 0.078125, ((0, 32), (2, 16)))
    w_up = gaussian(keys[4], (EXPERTS * GROUP, D, HID // GROUP), D ** -0.5, 0.078125, ((0, 32), (2, 16)))
    w_down = gaussian(keys[5], (EXPERTS * GROUP, HID // GROUP, D), HID ** -0.5, 0.0625, ((0, 32), (1, 16)))
    d_out = gaussian(keys[6], (TOKENS, D), 1.0, 6.0, ((0, 32), (1, 16)))
    return {"tokens": tokens, "expert_ids": expert_ids, "gates": gates, "w_gate": w_gate, "w_up": w_up, "w_down": w_down, "d_out": d_out}


def reference(tokens, expert_ids, gates, w_gate, w_up, w_down, d_out):
    blocks = N_EXPERT
    per_block = TOK_DEV * TOP
    ways = GROUP * N_PIPE * N_TENSOR
    block_hid = HID // ways
    group_hid = HID // GROUP
    full_gate = w_gate.reshape(EXPERTS, GROUP, D, group_hid).transpose(0, 2, 1, 3).reshape(EXPERTS, D, HID)
    full_up = w_up.reshape(EXPERTS, GROUP, D, group_hid).transpose(0, 2, 1, 3).reshape(EXPERTS, D, HID)
    full_down = w_down.reshape(EXPERTS, HID, D)
    flat = expert_ids.reshape(blocks, per_block)
    onehot = (flat[:, :, None] == jnp.arange(EXPERTS, dtype=jnp.int32)[None, None, :]).astype(jnp.int32)
    position = (jnp.sum(jnp.cumsum(onehot, axis=1) * onehot, axis=2) - 1).astype(jnp.int32)
    assign_index = jnp.arange(TOKENS * TOP, dtype=jnp.int32).reshape(blocks, per_block)
    block_index = jnp.broadcast_to(jnp.arange(blocks, dtype=jnp.int32)[:, None], (blocks, per_block))
    table = jnp.full((EXPERTS, blocks, CAP), -1, jnp.int32)
    table = table.at[flat, block_index, position].set(assign_index)
    table = table.reshape(EXPERTS, blocks * CAP)
    flat_gates = gates.reshape(-1)

    def expert(inputs):
        e_table, wg, wu, wd = inputs
        live = e_table >= 0
        safe = jnp.where(live, e_table, 0).astype(jnp.int32)
        tok_index = (safe // TOP).astype(jnp.int32)
        rows_x = tokens[tok_index] * live[:, None].astype(tokens.dtype)
        weight = jnp.where(live, flat_gates[safe], jnp.zeros((), flat_gates.dtype))
        rows_dy = (d_out[tok_index].astype(jnp.float32) * weight[:, None].astype(jnp.float32)).astype(jnp.bfloat16)
        h_gate = jnp.dot(rows_x, wg, preferred_element_type=jnp.float32)
        h_up = jnp.dot(rows_x, wu, preferred_element_type=jnp.float32)
        sig = jax.nn.sigmoid(h_gate)
        hidden = (h_gate * sig * h_up).astype(jnp.bfloat16)
        count = rows_x.shape[0]
        parts = jnp.einsum("rbh,bhd->brd", hidden.reshape(count, ways, block_hid).astype(jnp.float32),
                           wd.reshape(ways, block_hid, D).astype(jnp.float32), precision=lax.Precision.HIGHEST)
        parts = lax.optimization_barrier(parts.astype(jnp.bfloat16)).astype(jnp.float32)
        out = jnp.sum(parts, axis=0).astype(jnp.bfloat16)
        d_hidden = jnp.dot(rows_dy, wd.T, preferred_element_type=jnp.float32)
        d_gate_h = (d_hidden * h_up * sig * (1.0 + h_gate * (1.0 - sig))).astype(jnp.bfloat16)
        d_up_h = (d_hidden * h_gate * sig).astype(jnp.bfloat16)
        parts_dx = jnp.einsum("rbh,bhd->brd", d_gate_h.reshape(count, ways, block_hid).astype(jnp.float32),
                              wg.T.reshape(ways, block_hid, D).astype(jnp.float32), precision=lax.Precision.HIGHEST)
        parts_dx = parts_dx + jnp.einsum("rbh,bhd->brd", d_up_h.reshape(count, ways, block_hid).astype(jnp.float32),
                                         wu.T.reshape(ways, block_hid, D).astype(jnp.float32), precision=lax.Precision.HIGHEST)
        parts_dx = lax.optimization_barrier(parts_dx.astype(jnp.bfloat16)).astype(jnp.float32)
        grad_rows = jnp.sum(parts_dx, axis=0).astype(jnp.bfloat16)
        return out, grad_rows

    out_all, dx_all = lax.map(expert, (table, full_gate, full_up, full_down))
    slot_index = (block_index * CAP + position).reshape(-1).astype(jnp.int32)
    ids_flat = expert_ids.reshape(-1).astype(jnp.int32)
    a_out = out_all[ids_flat, slot_index].astype(jnp.float32).reshape(TOKENS, TOP, D)
    a_dx = dx_all[ids_flat, slot_index].astype(jnp.float32).reshape(TOKENS, TOP, D)
    moe_out = jnp.sum(gates[:, :, None].astype(jnp.float32) * a_out, axis=1).astype(jnp.bfloat16)
    grad_tokens = jnp.sum(a_dx, axis=1).astype(jnp.bfloat16)
    grad_gates = jnp.sum(d_out.astype(jnp.float32)[:, None, :] * a_out, axis=2)
    return moe_out, grad_tokens, grad_gates
```

```python
import jax
import jax.numpy as jnp
from jax import lax
from jax.sharding import PartitionSpec as P


def per_device(tokens, expert_ids, gates, w_gate, w_up, w_down, d_out):
    tok_rows = tokens.shape[0]
    feat = tokens.shape[1]
    top = expert_ids.shape[1]
    devices_all = lax.axis_size("expert")
    experts = min(8, devices_all)
    group = devices_all // experts
    capacity = min(
        tok_rows,
        max(2, max(5 * tok_rows * top // (4 * experts), (tok_rows * top + experts - 1) // experts)),
    )
    slots = experts * capacity
    flat_ids = expert_ids.reshape(-1)
    onehot = (flat_ids[:, None] == jnp.arange(experts, dtype=jnp.int32)[None, :]).astype(jnp.int32)
    position = jnp.sum(jnp.cumsum(onehot, axis=0) * onehot, axis=1) - 1
    slot_of = flat_ids * capacity + position
    picks = (jnp.arange(slots, dtype=jnp.int32)[:, None] == slot_of[None, :]).astype(jnp.float32)
    pick_rows = picks.reshape(slots, tok_rows, top)
    select_tok = jnp.sum(pick_rows, axis=2).astype(jnp.bfloat16)
    select_gate = jnp.sum(pick_rows * gates[None, :, :], axis=2)
    picked = jnp.dot(select_tok, tokens, preferred_element_type=jnp.float32).astype(jnp.bfloat16)
    scaled = jnp.dot(
        select_gate, d_out.astype(jnp.float32), precision=lax.Precision.HIGHEST
    ).astype(jnp.bfloat16)
    send = jnp.concatenate([picked, scaled], axis=1).reshape(experts, capacity, 2 * feat)
    send = jnp.repeat(send, group, axis=0)
    recv = lax.all_to_all(send, "expert", split_axis=0, concat_axis=0, tiled=True)
    recv = recv.reshape(devices_all * capacity, 2 * feat)
    part_x = recv[:, :feat]
    part_dy = recv[:, feat:]
    rows_x = lax.all_gather(part_x, ("pipe", "tensor"), axis=1, tiled=True)
    rows_dy = lax.all_gather(part_dy, ("pipe", "tensor"), axis=1, tiled=True)
    gate_proj = w_gate[0]
    up_proj = w_up[0]
    down_proj = w_down[0]
    contract_last = (((1,), (1,)), ((), ()))
    h_gate = jnp.dot(rows_x, gate_proj, preferred_element_type=jnp.float32)
    h_up = jnp.dot(rows_x, up_proj, preferred_element_type=jnp.float32)
    sig = jax.nn.sigmoid(h_gate)
    hidden = (h_gate * sig * h_up).astype(jnp.bfloat16)
    out_terms = jnp.dot(hidden, down_proj, preferred_element_type=jnp.float32)
    d_hidden = lax.dot_general(
        rows_dy, down_proj, contract_last, preferred_element_type=jnp.float32
    )
    d_gate_h = (d_hidden * h_up * sig * (1.0 + h_gate * (1.0 - sig))).astype(jnp.bfloat16)
    d_up_h = (d_hidden * h_gate * sig).astype(jnp.bfloat16)
    dx_terms = lax.dot_general(
        d_gate_h, gate_proj, contract_last, preferred_element_type=jnp.float32
    )
    dx_terms = dx_terms + lax.dot_general(
        d_up_h, up_proj, contract_last, preferred_element_type=jnp.float32
    )
    out_share = lax.psum_scatter(
        out_terms.astype(jnp.bfloat16), ("pipe", "tensor"), scatter_dimension=1, tiled=True
    )
    dx_share = lax.psum_scatter(
        dx_terms.astype(jnp.bfloat16), ("pipe", "tensor"), scatter_dimension=1, tiled=True
    )
    back_send = jnp.concatenate([out_share, dx_share], axis=1).reshape(
        devices_all, capacity, 2 * feat
    )
    back = lax.all_to_all(back_send, "expert", split_axis=0, concat_axis=0, tiled=True)
    back_rows = (
        jnp.sum(back.astype(jnp.float32).reshape(experts, group, capacity, 2 * feat), axis=1)
        .astype(jnp.bfloat16)
        .reshape(slots, 2 * feat)
    )
    assign = picks.T.astype(jnp.bfloat16)
    a_both = jnp.dot(assign, back_rows, preferred_element_type=jnp.float32)
    a_out = a_both[:, :feat].reshape(tok_rows, top, feat)
    a_dx = a_both[:, feat:].reshape(tok_rows, top, feat)
    moe_out = jnp.sum(gates[:, :, None] * a_out, axis=1).astype(jnp.bfloat16)
    grad_tokens = jnp.sum(a_dx, axis=1).astype(jnp.bfloat16)
    partial_dots = jnp.sum(d_out.astype(jnp.float32)[:, None, :] * a_out, axis=2)
    grad_gates = lax.psum(partial_dots, ("pipe", "tensor"))
    return (moe_out, grad_tokens, grad_gates)


def solution(mesh):
    return jax.shard_map(
        per_device,
        mesh=mesh,
        in_specs=(
            P("expert", ("pipe", "tensor")),
            P("expert", None),
            P("expert", None),
            P("expert", None, ("pipe", "tensor")),
            P("expert", None, ("pipe", "tensor")),
            P("expert", ("pipe", "tensor"), None),
            P("expert", ("pipe", "tensor")),
        ),
        out_specs=(
            P("expert", ("pipe", "tensor")),
            P("expert", ("pipe", "tensor")),
            P("expert", None),
        ),
        check_vma=False,
    )
```

```python
import jax
import jax.numpy as jnp
from jax import lax
from jax.sharding import PartitionSpec as P


def per_device(tokens, expert_ids, gates, w_gate, w_up, w_down, d_out):
    tok_rows = tokens.shape[0]
    feat = tokens.shape[1]
    top = expert_ids.shape[1]
    devices_all = lax.axis_size("expert")
    experts = min(8, devices_all)
    group = devices_all // experts
    capacity = min(
        tok_rows,
        max(2, max(5 * tok_rows * top // (4 * experts), (tok_rows * top + experts - 1) // experts)),
    )
    slots = experts * capacity
    flat_ids = expert_ids.reshape(-1)
    onehot = (flat_ids[:, None] == jnp.arange(experts, dtype=jnp.int32)[None, :]).astype(jnp.int32)
    position = jnp.sum(jnp.cumsum(onehot, axis=0) * onehot, axis=1) - 1
    slot_of = flat_ids * capacity + position
    picks = (jnp.arange(slots, dtype=jnp.int32)[:, None] == slot_of[None, :]).astype(jnp.float32)
    pick_rows = picks.reshape(slots, tok_rows, top)
    select_tok = jnp.sum(pick_rows, axis=2).astype(jnp.bfloat16)
    select_gate = jnp.sum(pick_rows * gates[None, :, :], axis=2)
    picked = jnp.dot(select_tok, tokens, preferred_element_type=jnp.float32).astype(jnp.bfloat16)
    scaled = jnp.dot(
        select_gate, d_out.astype(jnp.float32), precision=lax.Precision.HIGHEST
    ).astype(jnp.bfloat16)
    send = jnp.concatenate([picked, scaled], axis=1).reshape(experts, capacity, 2 * feat)
    send = jnp.repeat(send, group, axis=0)
    recv = lax.all_to_all(send, "expert", split_axis=0, concat_axis=0, tiled=True)
    recv = recv.reshape(devices_all * capacity, 2 * feat)
    planes = lax.axis_size("pipe") * lax.axis_size("tensor")
    spread = jnp.broadcast_to(recv[None], (planes,) + recv.shape)
    gathered = lax.all_to_all(spread, ("pipe", "tensor"), 0, 0, tiled=True)
    rows_x = gathered[:, :, :feat].transpose(1, 0, 2).reshape(devices_all * capacity, planes * feat)
    rows_dy = gathered[:, :, feat:].transpose(1, 0, 2).reshape(devices_all * capacity, planes * feat)
    gate_proj = w_gate[0]
    up_proj = w_up[0]
    down_proj = w_down[0]
    contract_last = (((1,), (1,)), ((), ()))
    h_gate = jnp.dot(rows_x, gate_proj, preferred_element_type=jnp.float32)
    h_up = jnp.dot(rows_x, up_proj, preferred_element_type=jnp.float32)
    sig = jax.nn.sigmoid(h_gate)
    hidden = (h_gate * sig * h_up).astype(jnp.bfloat16)
    out_terms = jnp.dot(hidden, down_proj, preferred_element_type=jnp.float32)
    d_hidden = lax.dot_general(
        rows_dy, down_proj, contract_last, preferred_element_type=jnp.float32
    )
    d_gate_h = (d_hidden * h_up * sig * (1.0 + h_gate * (1.0 - sig))).astype(jnp.bfloat16)
    d_up_h = (d_hidden * h_gate * sig).astype(jnp.bfloat16)
    dx_terms = lax.dot_general(
        d_gate_h, gate_proj, contract_last, preferred_element_type=jnp.float32
    )
    dx_terms = dx_terms + lax.dot_general(
        d_up_h, up_proj, contract_last, preferred_element_type=jnp.float32
    )
    rows_n = devices_all * capacity
    terms = jnp.concatenate(
        [
            out_terms.astype(jnp.bfloat16).reshape(rows_n, planes, feat),
            dx_terms.astype(jnp.bfloat16).reshape(rows_n, planes, feat),
        ],
        axis=2,
    ).transpose(1, 0, 2)
    reduced = lax.all_to_all(terms, ("pipe", "tensor"), 0, 0, tiled=True)
    shares = jnp.sum(reduced.astype(jnp.float32), axis=0).astype(jnp.bfloat16)
    back_send = shares.reshape(devices_all, capacity, 2 * feat)
    back = lax.all_to_all(back_send, "expert", split_axis=0, concat_axis=0, tiled=True)
    back_rows = (
        jnp.sum(back.astype(jnp.float32).reshape(experts, group, capacity, 2 * feat), axis=1)
        .astype(jnp.bfloat16)
        .reshape(slots, 2 * feat)
    )
    assign = picks.T.astype(jnp.bfloat16)
    a_both = jnp.dot(assign, back_rows, preferred_element_type=jnp.float32)
    a_out = a_both[:, :feat].reshape(tok_rows, top, feat)
    a_dx = a_both[:, feat:].reshape(tok_rows, top, feat)
    moe_out = jnp.sum(gates[:, :, None] * a_out, axis=1).astype(jnp.bfloat16)
    grad_tokens = jnp.sum(a_dx, axis=1).astype(jnp.bfloat16)
    partial_dots = jnp.sum(d_out.astype(jnp.float32)[:, None, :] * a_out, axis=2)
    grad_gates = lax.psum(partial_dots, ("pipe", "tensor"))
    return (moe_out, grad_tokens, grad_gates)


def solution(mesh):
    return jax.shard_map(
        per_device,
        mesh=mesh,
        in_specs=(
            P("expert", ("pipe", "tensor")),
            P("expert", None),
            P("expert", None),
            P("expert", None, ("pipe", "tensor")),
            P("expert", None, ("pipe", "tensor")),
            P("expert", ("pipe", "tensor"), None),
            P("expert", ("pipe", "tensor")),
        ),
        out_specs=(
            P("expert", ("pipe", "tensor")),
            P("expert", ("pipe", "tensor")),
            P("expert", None),
        ),
        check_vma=False,
    )
```

```python
import jax
import jax.numpy as jnp
from jax import lax
from jax.sharding import PartitionSpec as P


def per_device(tokens, expert_ids, gates, w_gate, w_up, w_down, d_out):
    tok_rows = tokens.shape[0]
    feat = tokens.shape[1]
    top = expert_ids.shape[1]
    devices_all = lax.axis_size("expert")
    experts = min(8, devices_all)
    group = devices_all // experts
    capacity = min(
        tok_rows,
        max(2, max(5 * tok_rows * top // (4 * experts), (tok_rows * top + experts - 1) // experts)),
    )
    slots = experts * capacity
    flat_ids = expert_ids.reshape(-1)
    onehot = (flat_ids[:, None] == jnp.arange(experts, dtype=jnp.int32)[None, :]).astype(jnp.int32)
    position = jnp.sum(jnp.cumsum(onehot, axis=0) * onehot, axis=1) - 1
    slot_of = flat_ids * capacity + position
    picks = (jnp.arange(slots, dtype=jnp.int32)[:, None] == slot_of[None, :]).astype(jnp.float32)
    pick_rows = picks.reshape(slots, tok_rows, top)
    select_tok = jnp.sum(pick_rows, axis=2).astype(jnp.bfloat16)
    select_gate = jnp.sum(pick_rows * gates[None, :, :], axis=2)
    picked = jnp.dot(select_tok, tokens, preferred_element_type=jnp.float32).astype(jnp.bfloat16)
    scaled = jnp.dot(
        select_gate, d_out.astype(jnp.float32), precision=lax.Precision.HIGHEST
    ).astype(jnp.bfloat16)
    send = jnp.concatenate([picked, scaled], axis=1).reshape(experts, capacity, 2 * feat)
    send = jnp.repeat(send, group, axis=0)
    recv = lax.all_to_all(send, "expert", split_axis=0, concat_axis=0, tiled=True)
    recv = recv.reshape(devices_all * capacity, 2 * feat)
    planes = lax.axis_size("pipe") * lax.axis_size("tensor")
    spread = jnp.broadcast_to(recv[None], (planes,) + recv.shape)
    gathered = lax.all_to_all(spread, ("pipe", "tensor"), 0, 0, tiled=True)
    rows_x = gathered[:, :, :feat].transpose(1, 0, 2).reshape(devices_all * capacity, planes * feat)
    rows_dy = gathered[:, :, feat:].transpose(1, 0, 2).reshape(devices_all * capacity, planes * feat)
    gate_proj = w_gate[0]
    up_proj = w_up[0]
    down_proj = w_down[0]
    contract_last = (((1,), (1,)), ((), ()))
    h_gate = jnp.dot(rows_x, gate_proj, preferred_element_type=jnp.float32)
    h_up = jnp.dot(rows_x, up_proj, preferred_element_type=jnp.float32)
    sig = jax.nn.sigmoid(h_gate)
    hidden = (h_gate * sig * h_up).astype(jnp.bfloat16)
    out_terms = jnp.dot(hidden, down_proj, preferred_element_type=jnp.float32)
    d_hidden = lax.dot_general(
        rows_dy, down_proj, contract_last, preferred_element_type=jnp.float32
    )
    d_gate_h = (d_hidden * h_up * sig * (1.0 + h_gate * (1.0 - sig))).astype(jnp.bfloat16)
    d_up_h = (d_hidden * h_gate * sig).astype(jnp.bfloat16)
    dx_terms = lax.dot_general(
        d_gate_h, gate_proj, contract_last, preferred_element_type=jnp.float32
    )
    dx_terms = dx_terms + lax.dot_general(
        d_up_h, up_proj, contract_last, preferred_element_type=jnp.float32
    )
    rows_n = devices_all * capacity
    terms = jnp.concatenate(
        [
            out_terms.astype(jnp.bfloat16).reshape(rows_n, planes, feat),
            dx_terms.astype(jnp.bfloat16).reshape(rows_n, planes, feat),
        ],
        axis=2,
    ).transpose(1, 0, 2)
    reduced = lax.all_to_all(terms, ("pipe", "tensor"), 0, 0, tiled=True)
    shares = jnp.sum(reduced.astype(jnp.float32), axis=0).astype(jnp.bfloat16)
    back_send = shares.reshape(devices_all, capacity, 2 * feat)
    back = lax.all_to_all(back_send, "expert", split_axis=0, concat_axis=0, tiled=True)
    back_rows = (
        jnp.sum(back.astype(jnp.float32).reshape(experts, group, capacity, 2 * feat), axis=1)
        .astype(jnp.bfloat16)
        .reshape(slots, 2 * feat)
    )
    assign = picks.T.astype(jnp.bfloat16)
    a_both = jnp.dot(assign, back_rows, preferred_element_type=jnp.float32)
    a_out = a_both[:, :feat].reshape(tok_rows, top, feat)
    a_dx = a_both[:, feat:].reshape(tok_rows, top, feat)
    moe_out = jnp.sum(gates[:, :, None] * a_out, axis=1).astype(jnp.bfloat16)
    grad_tokens = jnp.sum(a_dx, axis=1).astype(jnp.bfloat16)
    partial_dots = jnp.sum(d_out.astype(jnp.float32)[:, None, :] * a_out, axis=2)
    dots_spread = jnp.broadcast_to(partial_dots[None], (planes,) + partial_dots.shape)
    grad_gates = jnp.sum(lax.all_to_all(dots_spread, ("pipe", "tensor"), 0, 0, tiled=True), axis=0)
    return (moe_out, grad_tokens, grad_gates)


def solution(mesh):
    return jax.shard_map(
        per_device,
        mesh=mesh,
        in_specs=(
            P("expert", ("pipe", "tensor")),
            P("expert", None),
            P("expert", None),
            P("expert", None, ("pipe", "tensor")),
            P("expert", None, ("pipe", "tensor")),
            P("expert", ("pipe", "tensor"), None),
            P("expert", ("pipe", "tensor")),
        ),
        out_specs=(
            P("expert", ("pipe", "tensor")),
            P("expert", ("pipe", "tensor")),
            P("expert", None),
        ),
        check_vma=False,
    )
```

```python
import jax
import jax.numpy as jnp
from jax import lax
from jax.sharding import PartitionSpec as P


def per_device(tokens, expert_ids, gates, w_gate, w_up, w_down, d_out):
    tok_rows = tokens.shape[0]
    feat = tokens.shape[1]
    top = expert_ids.shape[1]
    devices_all = lax.axis_size("expert")
    planes = lax.axis_size("pipe") * lax.axis_size("tensor")
    experts = min(8, devices_all)
    group = devices_all // experts
    capacity = min(
        tok_rows,
        max(2, max(5 * tok_rows * top // (4 * experts), (tok_rows * top + experts - 1) // experts)),
    )
    slots = experts * capacity
    rows_n = devices_all * capacity
    core = lax.axis_index("expert") % 2
    first_core = core == 0
    partner = [(i, i ^ 1) for i in range(devices_all)]
    flat_ids = expert_ids.reshape(-1)
    onehot = (flat_ids[:, None] == jnp.arange(experts, dtype=jnp.int32)[None, :]).astype(jnp.int32)
    position = jnp.sum(jnp.cumsum(onehot, axis=0) * onehot, axis=1) - 1
    slot_of = flat_ids * capacity + position
    picks = (jnp.arange(slots, dtype=jnp.int32)[:, None] == slot_of[None, :]).astype(jnp.float32)
    pick_rows = picks.reshape(slots, tok_rows, top)
    select_tok = jnp.sum(pick_rows, axis=2).astype(jnp.bfloat16)
    select_gate = jnp.sum(pick_rows * gates[None, :, :], axis=2)
    picked = jnp.dot(select_tok, tokens, preferred_element_type=jnp.float32).astype(jnp.bfloat16)
    scaled = jnp.dot(
        select_gate, d_out.astype(jnp.float32), precision=lax.Precision.HIGHEST
    ).astype(jnp.bfloat16)
    pair = jnp.stack(
        [picked.reshape(experts, capacity, feat), scaled.reshape(experts, capacity, feat)], axis=1
    )
    send = jnp.concatenate([pair] * (group // 2), axis=1).reshape(devices_all, capacity, feat)
    recv = lax.all_to_all(send, "expert", split_axis=0, concat_axis=0, tiled=True)
    recv = recv.reshape(rows_n, feat)
    spread = jnp.broadcast_to(recv[None], (planes,) + recv.shape)
    gathered = lax.all_to_all(spread, ("pipe", "tensor"), 0, 0, tiled=True)
    own_rows = gathered.transpose(1, 0, 2).reshape(rows_n, planes * feat)
    other_rows = lax.ppermute(own_rows, "expert", partner)
    rows_x = jnp.where(first_core, own_rows, other_rows)
    rows_dy = jnp.where(first_core, other_rows, own_rows)
    gate_proj = w_gate[0]
    up_proj = w_up[0]
    down_proj = w_down[0]
    contract_last = (((1,), (1,)), ((), ()))
    h_gate = jnp.dot(rows_x, gate_proj, preferred_element_type=jnp.float32)
    h_up = jnp.dot(rows_x, up_proj, preferred_element_type=jnp.float32)
    sig = jax.nn.sigmoid(h_gate)
    hidden = (h_gate * sig * h_up).astype(jnp.bfloat16)
    out_terms = jnp.dot(hidden, down_proj, preferred_element_type=jnp.float32).astype(jnp.bfloat16)
    d_hidden = lax.dot_general(
        rows_dy, down_proj, contract_last, preferred_element_type=jnp.float32
    )
    d_gate_h = (d_hidden * h_up * sig * (1.0 + h_gate * (1.0 - sig))).astype(jnp.bfloat16)
    d_up_h = (d_hidden * h_gate * sig).astype(jnp.bfloat16)
    dx_terms = lax.dot_general(
        d_gate_h, gate_proj, contract_last, preferred_element_type=jnp.float32
    )
    dx_terms = dx_terms + lax.dot_general(
        d_up_h, up_proj, contract_last, preferred_element_type=jnp.float32
    )
    dx_terms = dx_terms.astype(jnp.bfloat16)
    keep = jnp.where(first_core, out_terms, dx_terms)
    give = jnp.where(first_core, dx_terms, out_terms)
    got = lax.ppermute(give, "expert", partner)
    both = (keep.astype(jnp.float32) + got.astype(jnp.float32)).astype(jnp.bfloat16)
    terms = both.reshape(rows_n, planes, feat).transpose(1, 0, 2)
    reduced = lax.all_to_all(terms, ("pipe", "tensor"), 0, 0, tiled=True)
    shares = jnp.sum(reduced.astype(jnp.float32), axis=0).astype(jnp.bfloat16)
    back_send = shares.reshape(devices_all, capacity, feat)
    back = lax.all_to_all(back_send, "expert", split_axis=0, concat_axis=0, tiled=True)
    back = back.astype(jnp.float32).reshape(experts, group // 2, 2, capacity, feat)
    back_rows = jnp.sum(back, axis=1).astype(jnp.bfloat16)
    back_rows = back_rows.transpose(0, 2, 1, 3).reshape(slots, 2 * feat)
    assign = picks.T.astype(jnp.bfloat16)
    a_both = jnp.dot(assign, back_rows, preferred_element_type=jnp.float32)
    a_out = a_both[:, :feat].reshape(tok_rows, top, feat)
    a_dx = a_both[:, feat:].reshape(tok_rows, top, feat)
    moe_out = jnp.sum(gates[:, :, None] * a_out, axis=1).astype(jnp.bfloat16)
    grad_tokens = jnp.sum(a_dx, axis=1).astype(jnp.bfloat16)
    partial_dots = jnp.sum(d_out.astype(jnp.float32)[:, None, :] * a_out, axis=2)
    dots_spread = jnp.broadcast_to(partial_dots[None], (planes,) + partial_dots.shape)
    grad_gates = jnp.sum(lax.all_to_all(dots_spread, ("pipe", "tensor"), 0, 0, tiled=True), axis=0)
    return (moe_out, grad_tokens, grad_gates)


def solution(mesh):
    return jax.shard_map(
        per_device,
        mesh=mesh,
        in_specs=(
            P("expert", ("pipe", "tensor")),
            P("expert", None),
            P("expert", None),
            P("expert", None, ("pipe", "tensor")),
            P("expert", None, ("pipe", "tensor")),
            P("expert", ("pipe", "tensor"), None),
            P("expert", ("pipe", "tensor")),
        ),
        out_specs=(
            P("expert", ("pipe", "tensor")),
            P("expert", ("pipe", "tensor")),
            P("expert", None),
        ),
        check_vma=False,
    )
```

```python
import jax
import jax.numpy as jnp
from jax import lax
from jax.sharding import PartitionSpec as P


def per_device(tokens, expert_ids, gates, w_gate, w_up, w_down, d_out):
    tok_rows = tokens.shape[0]
    feat = tokens.shape[1]
    top = expert_ids.shape[1]
    devices_all = lax.axis_size("expert")
    planes = lax.axis_size("pipe") * lax.axis_size("tensor")
    experts = min(8, devices_all)
    group = devices_all // experts
    capacity = min(
        tok_rows,
        max(2, max(5 * tok_rows * top // (4 * experts), (tok_rows * top + experts - 1) // experts)),
    )
    slots = experts * capacity
    rows_n = devices_all * capacity
    core = lax.axis_index("expert") % 2
    first_core = core == 0
    partner = [(i, i ^ 1) for i in range(devices_all)]
    flat_ids = expert_ids.reshape(-1)
    onehot = (flat_ids[:, None] == jnp.arange(experts, dtype=jnp.int32)[None, :]).astype(jnp.int32)
    position = jnp.sum(jnp.cumsum(onehot, axis=0) * onehot, axis=1) - 1
    slot_of = flat_ids * capacity + position
    picks = (jnp.arange(slots, dtype=jnp.int32)[:, None] == slot_of[None, :]).astype(jnp.float32)
    pick_rows = picks.reshape(slots, tok_rows, top)
    select_tok = jnp.sum(pick_rows, axis=2).astype(jnp.bfloat16)
    slot_gate = jnp.sum(pick_rows * gates[None, :, :], axis=(1, 2))
    both_in = jnp.concatenate([tokens, d_out], axis=1)
    chosen = jnp.dot(select_tok, both_in, preferred_element_type=jnp.float32)
    picked = chosen[:, :feat].astype(jnp.bfloat16)
    scaled = (chosen[:, feat:] * slot_gate[:, None]).astype(jnp.bfloat16)
    pair = jnp.stack(
        [picked.reshape(experts, capacity, feat), scaled.reshape(experts, capacity, feat)], axis=1
    )
    send = jnp.concatenate([pair] * (group // 2), axis=1).reshape(devices_all, capacity, feat)
    recv = lax.all_to_all(send, "expert", split_axis=0, concat_axis=0, tiled=True)
    recv = recv.reshape(rows_n, feat)
    spread = jnp.broadcast_to(recv[None], (planes,) + recv.shape)
    gathered = lax.all_to_all(spread, ("pipe", "tensor"), 0, 0, tiled=True)
    own_rows = gathered.transpose(1, 0, 2).reshape(rows_n, planes * feat)
    other_rows = lax.ppermute(own_rows, "expert", partner)
    rows_x = jnp.where(first_core, own_rows, other_rows)
    rows_dy = jnp.where(first_core, other_rows, own_rows)
    gate_proj = w_gate[0]
    up_proj = w_up[0]
    down_proj = w_down[0]
    contract_last = (((1,), (1,)), ((), ()))
    h_gate = jnp.dot(rows_x, gate_proj, preferred_element_type=jnp.float32)
    h_up = jnp.dot(rows_x, up_proj, preferred_element_type=jnp.float32)
    sig = jax.nn.sigmoid(h_gate)
    hidden = (h_gate * sig * h_up).astype(jnp.bfloat16)
    out_terms = jnp.dot(hidden, down_proj, preferred_element_type=jnp.float32).astype(jnp.bfloat16)
    d_hidden = lax.dot_general(
        rows_dy, down_proj, contract_last, preferred_element_type=jnp.float32
    )
    d_gate_h = (d_hidden * h_up * sig * (1.0 + h_gate * (1.0 - sig))).astype(jnp.bfloat16)
    d_up_h = (d_hidden * h_gate * sig).astype(jnp.bfloat16)
    dx_terms = lax.dot_general(
        d_gate_h, gate_proj, contract_last, preferred_element_type=jnp.float32
    )
    dx_terms = dx_terms + lax.dot_general(
        d_up_h, up_proj, contract_last, preferred_element_type=jnp.float32
    )
    dx_terms = dx_terms.astype(jnp.bfloat16)
    keep = jnp.where(first_core, out_terms, dx_terms)
    give = jnp.where(first_core, dx_terms, out_terms)
    got = lax.ppermute(give, "expert", partner)
    both = (keep.astype(jnp.float32) + got.astype(jnp.float32)).astype(jnp.bfloat16)
    terms = both.reshape(rows_n, planes, feat).transpose(1, 0, 2)
    reduced = lax.all_to_all(terms, ("pipe", "tensor"), 0, 0, tiled=True)
    shares = jnp.sum(reduced.astype(jnp.float32), axis=0).astype(jnp.bfloat16)
    back_send = shares.reshape(devices_all, capacity, feat)
    back = lax.all_to_all(back_send, "expert", split_axis=0, concat_axis=0, tiled=True)
    back = back.astype(jnp.float32).reshape(experts, group // 2, 2, capacity, feat)
    back_rows = jnp.sum(back, axis=1).astype(jnp.bfloat16)
    back_rows = back_rows.transpose(0, 2, 1, 3).reshape(slots, 2 * feat)
    assign = picks.T.astype(jnp.bfloat16)
    a_both = jnp.dot(assign, back_rows, preferred_element_type=jnp.float32)
    a_out = a_both[:, :feat].reshape(tok_rows, top, feat)
    a_dx = a_both[:, feat:].reshape(tok_rows, top, feat)
    moe_out = jnp.sum(gates[:, :, None] * a_out, axis=1).astype(jnp.bfloat16)
    grad_tokens = jnp.sum(a_dx, axis=1).astype(jnp.bfloat16)
    partial_dots = jnp.sum(d_out.astype(jnp.float32)[:, None, :] * a_out, axis=2)
    dots_spread = jnp.broadcast_to(partial_dots[None], (planes,) + partial_dots.shape)
    grad_gates = jnp.sum(lax.all_to_all(dots_spread, ("pipe", "tensor"), 0, 0, tiled=True), axis=0)
    return (moe_out, grad_tokens, grad_gates)


def solution(mesh):
    return jax.shard_map(
        per_device,
        mesh=mesh,
        in_specs=(
            P("expert", ("pipe", "tensor")),
            P("expert", None),
            P("expert", None),
            P("expert", None, ("pipe", "tensor")),
            P("expert", None, ("pipe", "tensor")),
            P("expert", ("pipe", "tensor"), None),
            P("expert", ("pipe", "tensor")),
        ),
        out_specs=(
            P("expert", ("pipe", "tensor")),
            P("expert", ("pipe", "tensor")),
            P("expert", None),
        ),
        check_vma=False,
    )
```

```python
import jax
import jax.numpy as jnp
from jax import lax
from jax.sharding import PartitionSpec as P


def per_device(tokens, expert_ids, gates, w_gate, w_up, w_down, d_out):
    tok_rows = tokens.shape[0]
    feat = tokens.shape[1]
    top = expert_ids.shape[1]
    devices_all = lax.axis_size("expert")
    planes = lax.axis_size("pipe") * lax.axis_size("tensor")
    experts = min(8, devices_all)
    group = devices_all // experts
    capacity = min(
        tok_rows,
        max(2, max(5 * tok_rows * top // (4 * experts), (tok_rows * top + experts - 1) // experts)),
    )
    slots = experts * capacity
    rows_n = devices_all * capacity
    core = lax.axis_index("expert") % 2
    first_core = core == 0
    partner = [(i, i ^ 1) for i in range(devices_all)]
    flat_ids = expert_ids.reshape(-1)
    onehot = (flat_ids[:, None] == jnp.arange(experts, dtype=jnp.int32)[None, :]).astype(jnp.int32)
    position = jnp.sum(jnp.cumsum(onehot, axis=0) * onehot, axis=1) - 1
    slot_of = flat_ids * capacity + position
    picks = (jnp.arange(slots, dtype=jnp.int32)[:, None] == slot_of[None, :]).astype(jnp.float32)
    pick_rows = picks.reshape(slots, tok_rows, top)
    select_tok = jnp.sum(pick_rows, axis=2).astype(jnp.bfloat16)
    slot_gate = jnp.sum(pick_rows * gates[None, :, :], axis=(1, 2))
    both_in = jnp.concatenate([tokens, d_out], axis=1)
    chosen = jnp.dot(select_tok, both_in, preferred_element_type=jnp.float32)
    picked = chosen[:, :feat].astype(jnp.bfloat16)
    scaled = (chosen[:, feat:] * slot_gate[:, None]).astype(jnp.bfloat16)
    pair = jnp.stack(
        [picked.reshape(experts, capacity, feat), scaled.reshape(experts, capacity, feat)], axis=1
    )
    send = jnp.concatenate([pair] * (group // 2), axis=1).reshape(devices_all, capacity, feat)
    recv = lax.all_to_all(send, "expert", split_axis=0, concat_axis=0, tiled=True)
    recv = recv.reshape(rows_n, feat)
    spread = jnp.broadcast_to(recv[None], (planes,) + recv.shape)
    gathered = lax.all_to_all(spread, ("pipe", "tensor"), 0, 0, tiled=True)
    own_rows = gathered.transpose(1, 0, 2).reshape(rows_n, planes * feat)
    other_rows = lax.ppermute(own_rows, "expert", partner)
    rows_x = jnp.where(first_core, own_rows, other_rows)
    rows_dy = jnp.where(first_core, other_rows, own_rows)
    gate_proj = w_gate[0]
    up_proj = w_up[0]
    down_proj = w_down[0]
    contract_last = (((1,), (1,)), ((), ()))
    h_gate = jnp.dot(rows_x, gate_proj, preferred_element_type=jnp.float32)
    h_up = jnp.dot(rows_x, up_proj, preferred_element_type=jnp.float32)
    sig = jax.nn.sigmoid(h_gate)
    hidden = (h_gate * sig * h_up).astype(jnp.bfloat16)
    out_terms = jnp.dot(hidden, down_proj, preferred_element_type=jnp.float32).astype(jnp.bfloat16)
    d_hidden = lax.dot_general(
        rows_dy, down_proj, contract_last, preferred_element_type=jnp.float32
    )
    d_gate_h = (d_hidden * h_up * sig * (1.0 + h_gate * (1.0 - sig))).astype(jnp.bfloat16)
    d_up_h = (d_hidden * h_gate * sig).astype(jnp.bfloat16)
    dx_terms = lax.dot_general(
        d_gate_h, gate_proj, contract_last, preferred_element_type=jnp.float32
    )
    dx_terms = dx_terms + lax.dot_general(
        d_up_h, up_proj, contract_last, preferred_element_type=jnp.float32
    )
    dx_terms = dx_terms.astype(jnp.bfloat16)
    keep = jnp.where(first_core, out_terms, dx_terms)
    give = jnp.where(first_core, dx_terms, out_terms)
    got = lax.ppermute(give, "expert", partner)
    both_f32 = keep.astype(jnp.float32) + got.astype(jnp.float32)
    both = both_f32.astype(jnp.bfloat16)
    row_dots = jnp.sum(rows_dy.astype(jnp.float32) * both_f32, axis=1)
    dots_hi = row_dots.astype(jnp.bfloat16)
    dots_lo = (row_dots - dots_hi.astype(jnp.float32)).astype(jnp.bfloat16)
    dots_row = jnp.concatenate(
        [dots_hi, dots_lo, jnp.zeros((feat - 2 * rows_n,), jnp.bfloat16)]
    ).reshape(1, 1, feat)
    terms = both.reshape(rows_n, planes, feat).transpose(1, 0, 2)
    terms = jnp.concatenate([terms, jnp.broadcast_to(dots_row, (planes, 1, feat))], axis=1)
    reduced = lax.all_to_all(terms, ("pipe", "tensor"), 0, 0, tiled=True).astype(jnp.float32)
    shares = jnp.sum(reduced[:, :rows_n], axis=0).astype(jnp.bfloat16)
    dots_sum = jnp.sum(reduced[:, rows_n, :rows_n] + reduced[:, rows_n, rows_n:2 * rows_n], axis=0)
    back_hi = dots_sum.astype(jnp.bfloat16)
    back_lo = (dots_sum - back_hi.astype(jnp.float32)).astype(jnp.bfloat16)
    back_dots = jnp.concatenate(
        [
            back_hi.reshape(devices_all, capacity),
            back_lo.reshape(devices_all, capacity),
            jnp.zeros((devices_all, feat - 2 * capacity), jnp.bfloat16),
        ],
        axis=1,
    ).reshape(devices_all, 1, feat)
    back_send = jnp.concatenate([shares.reshape(devices_all, capacity, feat), back_dots], axis=1)
    back = lax.all_to_all(back_send, "expert", split_axis=0, concat_axis=0, tiled=True)
    back = back.astype(jnp.float32).reshape(experts, group // 2, 2, capacity + 1, feat)
    back_rows = jnp.sum(back[:, :, :, :capacity], axis=1).astype(jnp.bfloat16)
    back_rows = back_rows.transpose(0, 2, 1, 3).reshape(slots, 2 * feat)
    slot_dots = jnp.sum(
        back[:, :, 0, capacity, :capacity] + back[:, :, 0, capacity, capacity:2 * capacity], axis=1
    ).reshape(slots)
    assign = picks.T.astype(jnp.bfloat16)
    a_both = jnp.dot(assign, back_rows, preferred_element_type=jnp.float32)
    a_out = a_both[:, :feat].reshape(tok_rows, top, feat)
    a_dx = a_both[:, feat:].reshape(tok_rows, top, feat)
    moe_out = jnp.sum(gates[:, :, None] * a_out, axis=1).astype(jnp.bfloat16)
    grad_tokens = jnp.sum(a_dx, axis=1).astype(jnp.bfloat16)
    assign_dots = jnp.sum(picks.T * slot_dots[None, :], axis=1).reshape(tok_rows, top)
    grad_gates = assign_dots / gates
    return (moe_out, grad_tokens, grad_gates)


def solution(mesh):
    return jax.shard_map(
        per_device,
        mesh=mesh,
        in_specs=(
            P("expert", ("pipe", "tensor")),
            P("expert", None),
            P("expert", None),
            P("expert", None, ("pipe", "tensor")),
            P("expert", None, ("pipe", "tensor")),
            P("expert", ("pipe", "tensor"), None),
            P("expert", ("pipe", "tensor")),
        ),
        out_specs=(
            P("expert", ("pipe", "tensor")),
            P("expert", ("pipe", "tensor")),
            P("expert", None),
        ),
        check_vma=False,
    )
```

```python
import jax
import jax.numpy as jnp
from jax import lax
from jax.sharding import PartitionSpec as P


def per_device(tokens, expert_ids, gates, w_gate, w_up, w_down, d_out):
    tok_rows = tokens.shape[0]
    feat = tokens.shape[1]
    top = expert_ids.shape[1]
    devices_all = lax.axis_size("expert")
    planes = lax.axis_size("pipe") * lax.axis_size("tensor")
    experts = min(8, devices_all)
    group = devices_all // experts
    capacity = min(
        tok_rows,
        max(2, max(5 * tok_rows * top // (4 * experts), (tok_rows * top + experts - 1) // experts)),
    )
    slots = experts * capacity
    rows_n = devices_all * capacity
    core = lax.axis_index("expert") % 2
    first_core = core == 0
    partner = [(i, i ^ 1) for i in range(devices_all)]
    flat_ids = expert_ids.reshape(-1)
    onehot = (flat_ids[:, None] == jnp.arange(experts, dtype=jnp.int32)[None, :]).astype(jnp.int32)
    position = jnp.sum(jnp.cumsum(onehot, axis=0) * onehot, axis=1) - 1
    slot_of = flat_ids * capacity + position
    picks = (jnp.arange(slots, dtype=jnp.int32)[:, None] == slot_of[None, :]).astype(jnp.float32)
    pick_rows = picks.reshape(slots, tok_rows, top)
    select_tok = jnp.sum(pick_rows, axis=2).astype(jnp.bfloat16)
    slot_gate = jnp.sum(pick_rows * gates[None, :, :], axis=(1, 2))
    both_in = jnp.concatenate([tokens, d_out], axis=1)
    chosen = jnp.dot(select_tok, both_in, preferred_element_type=jnp.float32)
    picked = chosen[:, :feat].astype(jnp.bfloat16)
    scaled = (chosen[:, feat:] * slot_gate[:, None]).astype(jnp.bfloat16)
    pair = jnp.stack(
        [picked.reshape(experts, capacity, feat), scaled.reshape(experts, capacity, feat)], axis=1
    )
    send = jnp.concatenate([pair] * (group // 2), axis=1).reshape(devices_all, capacity, feat)
    recv = lax.all_to_all(send, "expert", split_axis=0, concat_axis=0, tiled=True)
    recv = recv.reshape(rows_n, feat)
    spread = jnp.broadcast_to(recv[None], (planes,) + recv.shape)
    gathered = lax.all_to_all(spread, ("pipe", "tensor"), 0, 0, tiled=True)
    own_rows = gathered.transpose(1, 0, 2).reshape(rows_n, planes * feat)
    other_rows = lax.ppermute(own_rows, "expert", partner)
    rows_x = jnp.where(first_core, own_rows, other_rows)
    rows_dy = jnp.where(first_core, other_rows, own_rows)
    gate_proj = w_gate[0]
    up_proj = w_up[0]
    down_proj = w_down[0]
    contract_last = (((1,), (1,)), ((), ()))
    h_gate = jnp.dot(rows_x, gate_proj, preferred_element_type=jnp.float32)
    h_up = jnp.dot(rows_x, up_proj, preferred_element_type=jnp.float32)
    sig = jax.nn.sigmoid(h_gate)
    hidden = (h_gate * sig * h_up).astype(jnp.bfloat16)
    out_terms = jnp.dot(hidden, down_proj, preferred_element_type=jnp.float32).astype(jnp.bfloat16)
    d_hidden = lax.dot_general(
        rows_dy, down_proj, contract_last, preferred_element_type=jnp.float32
    )
    d_gate_h = (d_hidden * h_up * sig * (1.0 + h_gate * (1.0 - sig))).astype(jnp.bfloat16)
    d_up_h = (d_hidden * h_gate * sig).astype(jnp.bfloat16)
    dx_terms = lax.dot_general(
        d_gate_h, gate_proj, contract_last, preferred_element_type=jnp.float32
    )
    dx_terms = dx_terms + lax.dot_general(
        d_up_h, up_proj, contract_last, preferred_element_type=jnp.float32
    )
    dx_terms = dx_terms.astype(jnp.bfloat16)
    row_dots = jnp.sum(rows_dy.astype(jnp.float32) * out_terms.astype(jnp.float32), axis=1)
    dots_hi = row_dots.astype(jnp.bfloat16)
    dots_lo = (row_dots - dots_hi.astype(jnp.float32)).astype(jnp.bfloat16)
    dots_row = jnp.concatenate(
        [dots_hi, dots_lo, jnp.zeros((feat - 2 * rows_n,), jnp.bfloat16)]
    ).reshape(1, 1, feat)
    keep = jnp.where(first_core, out_terms, dx_terms)
    give = jnp.where(first_core, dx_terms, out_terms)
    got = lax.ppermute(give, "expert", partner)
    both = (keep.astype(jnp.float32) + got.astype(jnp.float32)).astype(jnp.bfloat16)
    terms = both.reshape(rows_n, planes, feat).transpose(1, 0, 2)
    terms = jnp.concatenate([terms, jnp.broadcast_to(dots_row, (planes, 1, feat))], axis=1)
    reduced = lax.all_to_all(terms, ("pipe", "tensor"), 0, 0, tiled=True)
    shares = jnp.sum(reduced[:, :rows_n].astype(jnp.float32), axis=0).astype(jnp.bfloat16)
    dots_in = reduced[:, rows_n, : 2 * rows_n].astype(jnp.float32)
    dots_sum = jnp.sum(dots_in[:, :rows_n] + dots_in[:, rows_n:], axis=0)
    back_hi = dots_sum.astype(jnp.bfloat16)
    back_lo = (dots_sum - back_hi.astype(jnp.float32)).astype(jnp.bfloat16)
    back_dots = jnp.concatenate(
        [
            back_hi.reshape(devices_all, capacity),
            back_lo.reshape(devices_all, capacity),
            jnp.zeros((devices_all, feat - 2 * capacity), jnp.bfloat16),
        ],
        axis=1,
    ).reshape(devices_all, 1, feat)
    back_send = jnp.concatenate([shares.reshape(devices_all, capacity, feat), back_dots], axis=1)
    back = lax.all_to_all(back_send, "expert", split_axis=0, concat_axis=0, tiled=True)
    back = back.reshape(experts, group // 2, 2, capacity + 1, feat)
    back_rows = jnp.sum(back[:, :, :, :capacity].astype(jnp.float32), axis=1).astype(jnp.bfloat16)
    back_rows = back_rows.transpose(0, 2, 1, 3).reshape(slots, 2 * feat)
    back_dots = back[:, :, :, capacity, : 2 * capacity].astype(jnp.float32)
    slot_dots = jnp.sum(
        back_dots[..., :capacity] + back_dots[..., capacity:], axis=(1, 2)
    ).reshape(slots)
    assign = picks.T.astype(jnp.bfloat16)
    a_both = jnp.dot(assign, back_rows, preferred_element_type=jnp.float32)
    a_out = a_both[:, :feat].reshape(tok_rows, top, feat)
    a_dx = a_both[:, feat:].reshape(tok_rows, top, feat)
    moe_out = jnp.sum(gates[:, :, None] * a_out, axis=1).astype(jnp.bfloat16)
    grad_tokens = jnp.sum(a_dx, axis=1).astype(jnp.bfloat16)
    assign_dots = jnp.sum(picks.T * slot_dots[None, :], axis=1).reshape(tok_rows, top)
    grad_gates = assign_dots / gates
    return (moe_out, grad_tokens, grad_gates)


def solution(mesh):
    return jax.shard_map(
        per_device,
        mesh=mesh,
        in_specs=(
            P("expert", ("pipe", "tensor")),
            P("expert", None),
            P("expert", None),
            P("expert", None, ("pipe", "tensor")),
            P("expert", None, ("pipe", "tensor")),
            P("expert", ("pipe", "tensor"), None),
            P("expert", ("pipe", "tensor")),
        ),
        out_specs=(
            P("expert", ("pipe", "tensor")),
            P("expert", ("pipe", "tensor")),
            P("expert", None),
        ),
        check_vma=False,
    )
```

```python
import jax
import jax.numpy as jnp
from jax import lax
from jax.sharding import PartitionSpec as P


def per_device(tokens, expert_ids, gates, w_gate, w_up, w_down, d_out):
    tok_rows = tokens.shape[0]
    feat = tokens.shape[1]
    top = expert_ids.shape[1]
    devices_all = lax.axis_size("expert")
    planes = lax.axis_size("pipe") * lax.axis_size("tensor")
    experts = min(8, devices_all)
    group = devices_all // experts
    capacity = min(
        tok_rows,
        max(2, max(5 * tok_rows * top // (4 * experts), (tok_rows * top + experts - 1) // experts)),
    )
    slots = experts * capacity
    rows_n = devices_all * capacity
    core = lax.axis_index("expert") % 2
    first_core = core == 0
    partner = [(i, i ^ 1) for i in range(devices_all)]
    flat_ids = expert_ids.reshape(-1)
    onehot = (flat_ids[:, None] == jnp.arange(experts, dtype=jnp.int32)[None, :]).astype(jnp.int32)
    position = jnp.sum(jnp.cumsum(onehot, axis=0) * onehot, axis=1) - 1
    slot_of = flat_ids * capacity + position
    picks = (jnp.arange(slots, dtype=jnp.int32)[:, None] == slot_of[None, :]).astype(jnp.float32)
    pick_rows = picks.reshape(slots, tok_rows, top)
    select_tok = jnp.sum(pick_rows, axis=2).astype(jnp.bfloat16)
    slot_gate = jnp.sum(pick_rows * gates[None, :, :], axis=(1, 2))
    both_in = jnp.concatenate([tokens, d_out], axis=1)
    chosen = jnp.dot(select_tok, both_in, preferred_element_type=jnp.float32)
    picked = chosen[:, :feat].astype(jnp.bfloat16)
    scaled = (chosen[:, feat:] * slot_gate[:, None]).astype(jnp.bfloat16)
    pair = jnp.stack(
        [picked.reshape(experts, capacity, feat), scaled.reshape(experts, capacity, feat)], axis=1
    )
    send = jnp.concatenate([pair] * (group // 2), axis=1).reshape(devices_all, capacity, feat)
    recv = lax.all_to_all(send, "expert", split_axis=0, concat_axis=0, tiled=True)
    recv = recv.reshape(rows_n, feat)
    spread = jnp.broadcast_to(recv[None], (planes,) + recv.shape)
    gathered = lax.all_to_all(spread, ("pipe", "tensor"), 0, 0, tiled=True)
    own_rows = gathered.transpose(1, 0, 2).reshape(rows_n, planes * feat)
    other_rows = lax.ppermute(own_rows, "expert", partner)
    rows_x = jnp.where(first_core, own_rows, other_rows)
    rows_dy = jnp.where(first_core, other_rows, own_rows)
    gate_proj = w_gate[0]
    up_proj = w_up[0]
    down_proj = w_down[0]
    contract_last = (((1,), (1,)), ((), ()))
    h_gate = jnp.dot(rows_x, gate_proj, preferred_element_type=jnp.float32)
    h_up = jnp.dot(rows_x, up_proj, preferred_element_type=jnp.float32)
    sig = jax.nn.sigmoid(h_gate)
    hidden = (h_gate * sig * h_up).astype(jnp.bfloat16)
    out_terms = jnp.dot(hidden, down_proj, preferred_element_type=jnp.float32).astype(jnp.bfloat16)
    d_hidden = lax.dot_general(
        rows_dy, down_proj, contract_last, preferred_element_type=jnp.float32
    )
    d_gate_h = (d_hidden * h_up * sig * (1.0 + h_gate * (1.0 - sig))).astype(jnp.bfloat16)
    d_up_h = (d_hidden * h_gate * sig).astype(jnp.bfloat16)
    dx_terms = lax.dot_general(
        d_gate_h, gate_proj, contract_last, preferred_element_type=jnp.float32
    )
    dx_terms = dx_terms + lax.dot_general(
        d_up_h, up_proj, contract_last, preferred_element_type=jnp.float32
    )
    dx_terms = dx_terms.astype(jnp.bfloat16)
    row_dots = jnp.sum(hidden.astype(jnp.float32) * d_hidden, axis=1)
    dots_hi = row_dots.astype(jnp.bfloat16)
    dots_lo = (row_dots - dots_hi.astype(jnp.float32)).astype(jnp.bfloat16)
    dots_row = jnp.concatenate(
        [dots_hi, dots_lo, jnp.zeros((feat - 2 * rows_n,), jnp.bfloat16)]
    ).reshape(1, 1, feat)
    keep = jnp.where(first_core, out_terms, dx_terms)
    give = jnp.where(first_core, dx_terms, out_terms)
    got = lax.ppermute(give, "expert", partner)
    dots_line = jnp.broadcast_to(dots_row.reshape(1, feat), (planes, feat)).reshape(1, planes * feat)
    keep = jnp.concatenate([keep, dots_line], axis=0)
    got = jnp.concatenate([got, jnp.zeros((1, planes * feat), jnp.bfloat16)], axis=0)
    both = (keep.astype(jnp.float32) + got.astype(jnp.float32)).astype(jnp.bfloat16)
    terms = both.reshape(rows_n + 1, planes, feat).transpose(1, 0, 2)
    reduced = lax.all_to_all(terms, ("pipe", "tensor"), 0, 0, tiled=True)
    shares = jnp.sum(reduced[:, :rows_n].astype(jnp.float32), axis=0).astype(jnp.bfloat16)
    dots_in = reduced[:, rows_n, : 2 * rows_n].astype(jnp.float32)
    dots_sum = jnp.sum(dots_in[:, :rows_n] + dots_in[:, rows_n:], axis=0)
    back_hi = dots_sum.astype(jnp.bfloat16)
    back_lo = (dots_sum - back_hi.astype(jnp.float32)).astype(jnp.bfloat16)
    back_dots = jnp.concatenate(
        [
            back_hi.reshape(devices_all, capacity),
            back_lo.reshape(devices_all, capacity),
            jnp.zeros((devices_all, feat - 2 * capacity), jnp.bfloat16),
        ],
        axis=1,
    ).reshape(devices_all, 1, feat)
    back_send = jnp.concatenate([shares.reshape(devices_all, capacity, feat), back_dots], axis=1)
    back = lax.all_to_all(back_send, "expert", split_axis=0, concat_axis=0, tiled=True)
    back = back.reshape(experts, group // 2, 2, capacity + 1, feat)
    back_rows = jnp.sum(back[:, :, :, :capacity].astype(jnp.float32), axis=1).astype(jnp.bfloat16)
    back_rows = back_rows.transpose(0, 2, 1, 3).reshape(slots, 2 * feat)
    back_dots = back[:, :, :, capacity, : 2 * capacity].astype(jnp.float32)
    slot_dots = jnp.sum(
        back_dots[..., :capacity] + back_dots[..., capacity:], axis=(1, 2)
    ).reshape(slots)
    assign = picks.T.astype(jnp.bfloat16)
    a_both = jnp.dot(assign, back_rows, preferred_element_type=jnp.float32)
    a_out = a_both[:, :feat].reshape(tok_rows, top, feat)
    a_dx = a_both[:, feat:].reshape(tok_rows, top, feat)
    moe_out = jnp.sum(gates[:, :, None] * a_out, axis=1).astype(jnp.bfloat16)
    grad_tokens = jnp.sum(a_dx, axis=1).astype(jnp.bfloat16)
    assign_dots = jnp.sum(picks.T * slot_dots[None, :], axis=1).reshape(tok_rows, top)
    grad_gates = assign_dots / gates
    return (moe_out, grad_tokens, grad_gates)


def solution(mesh):
    return jax.shard_map(
        per_device,
        mesh=mesh,
        in_specs=(
            P("expert", ("pipe", "tensor")),
            P("expert", None),
            P("expert", None),
            P("expert", None, ("pipe", "tensor")),
            P("expert", None, ("pipe", "tensor")),
            P("expert", ("pipe", "tensor"), None),
            P("expert", ("pipe", "tensor")),
        ),
        out_specs=(
            P("expert", ("pipe", "tensor")),
            P("expert", ("pipe", "tensor")),
            P("expert", None),
        ),
        check_vma=False,
    )
```

```python
import jax
import jax.numpy as jnp
from jax import lax
from jax.sharding import PartitionSpec as P


def per_device(tokens, expert_ids, gates, w_gate, w_up, w_down, d_out):
    tok_rows = tokens.shape[0]
    feat = tokens.shape[1]
    top = expert_ids.shape[1]
    devices_all = lax.axis_size("expert")
    planes = lax.axis_size("pipe") * lax.axis_size("tensor")
    experts = min(8, devices_all)
    group = devices_all // experts
    capacity = min(
        tok_rows,
        max(2, max(5 * tok_rows * top // (4 * experts), (tok_rows * top + experts - 1) // experts)),
    )
    slots = experts * capacity
    rows_n = devices_all * capacity
    core = lax.axis_index("expert") % 2
    first_core = core == 0
    partner = [(i, i ^ 1) for i in range(devices_all)]
    flat_ids = expert_ids.reshape(-1)
    onehot = (flat_ids[:, None] == jnp.arange(experts, dtype=jnp.int32)[None, :]).astype(jnp.int32)
    position = jnp.sum(jnp.cumsum(onehot, axis=0) * onehot, axis=1) - 1
    slot_of = flat_ids * capacity + position
    picks = (jnp.arange(slots, dtype=jnp.int32)[:, None] == slot_of[None, :]).astype(jnp.float32)
    pick_rows = picks.reshape(slots, tok_rows, top)
    select_tok = jnp.sum(pick_rows, axis=2).astype(jnp.bfloat16)
    slot_gate = jnp.sum(pick_rows * gates[None, :, :], axis=(1, 2))
    both_in = jnp.concatenate([tokens, d_out], axis=1)
    chosen = jnp.dot(select_tok, both_in, preferred_element_type=jnp.float32)
    picked = chosen[:, :feat].astype(jnp.bfloat16)
    scaled = (chosen[:, feat:] * slot_gate[:, None]).astype(jnp.bfloat16)
    pair = jnp.stack(
        [picked.reshape(experts, capacity, feat), scaled.reshape(experts, capacity, feat)], axis=1
    )
    send = jnp.concatenate([pair] * (group // 2), axis=1).reshape(devices_all, capacity, feat)
    recv = lax.all_to_all(send, "expert", split_axis=0, concat_axis=0, tiled=True)
    recv = recv.reshape(rows_n, feat)
    spread = jnp.broadcast_to(recv[None], (planes,) + recv.shape)
    gathered = lax.all_to_all(spread, ("pipe", "tensor"), 0, 0, tiled=True)
    own_rows = gathered.transpose(1, 0, 2).reshape(rows_n, planes * feat)
    other_rows = lax.ppermute(own_rows, "expert", partner)
    rows_x = jnp.where(first_core, own_rows, other_rows)
    rows_dy = jnp.where(first_core, other_rows, own_rows)
    rows_x, rows_dy = lax.optimization_barrier((rows_x, rows_dy))
    gate_proj = w_gate[0]
    up_proj = w_up[0]
    down_proj = w_down[0]
    contract_last = (((1,), (1,)), ((), ()))
    h_gate = jnp.dot(rows_x, gate_proj, preferred_element_type=jnp.float32)
    h_up = jnp.dot(rows_x, up_proj, preferred_element_type=jnp.float32)
    sig = jax.nn.sigmoid(h_gate)
    hidden = (h_gate * sig * h_up).astype(jnp.bfloat16)
    out_terms = jnp.dot(hidden, down_proj, preferred_element_type=jnp.float32).astype(jnp.bfloat16)
    d_hidden = lax.dot_general(
        rows_dy, down_proj, contract_last, preferred_element_type=jnp.float32
    )
    d_gate_h = (d_hidden * h_up * sig * (1.0 + h_gate * (1.0 - sig))).astype(jnp.bfloat16)
    d_up_h = (d_hidden * h_gate * sig).astype(jnp.bfloat16)
    dx_terms = lax.dot_general(
        d_gate_h, gate_proj, contract_last, preferred_element_type=jnp.float32
    )
    dx_terms = dx_terms + lax.dot_general(
        d_up_h, up_proj, contract_last, preferred_element_type=jnp.float32
    )
    dx_terms = dx_terms.astype(jnp.bfloat16)
    keep = jnp.where(first_core, out_terms, dx_terms)
    give = jnp.where(first_core, dx_terms, out_terms)
    got = lax.ppermute(give, "expert", partner)
    both_f32 = keep.astype(jnp.float32) + got.astype(jnp.float32)
    both = both_f32.astype(jnp.bfloat16)
    row_dots = jnp.sum(rows_dy.astype(jnp.float32) * both_f32, axis=1)
    dots_hi = row_dots.astype(jnp.bfloat16)
    dots_lo = (row_dots - dots_hi.astype(jnp.float32)).astype(jnp.bfloat16)
    dots_row = jnp.concatenate(
        [dots_hi, dots_lo, jnp.zeros((feat - 2 * rows_n,), jnp.bfloat16)]
    ).reshape(1, 1, feat)
    terms = both.reshape(rows_n, planes, feat).transpose(1, 0, 2)
    terms = jnp.concatenate([terms, jnp.broadcast_to(dots_row, (planes, 1, feat))], axis=1)
    reduced = lax.all_to_all(terms, ("pipe", "tensor"), 0, 0, tiled=True).astype(jnp.float32)
    shares = jnp.sum(reduced[:, :rows_n], axis=0).astype(jnp.bfloat16)
    dots_sum = jnp.sum(reduced[:, rows_n, :rows_n] + reduced[:, rows_n, rows_n:2 * rows_n], axis=0)
    back_hi = dots_sum.astype(jnp.bfloat16)
    back_lo = (dots_sum - back_hi.astype(jnp.float32)).astype(jnp.bfloat16)
    back_dots = jnp.concatenate(
        [
            back_hi.reshape(devices_all, capacity),
            back_lo.reshape(devices_all, capacity),
            jnp.zeros((devices_all, feat - 2 * capacity), jnp.bfloat16),
        ],
        axis=1,
    ).reshape(devices_all, 1, feat)
    back_send = jnp.concatenate([shares.reshape(devices_all, capacity, feat), back_dots], axis=1)
    back = lax.all_to_all(back_send, "expert", split_axis=0, concat_axis=0, tiled=True)
    back = back.astype(jnp.float32).reshape(experts, group // 2, 2, capacity + 1, feat)
    back_rows = jnp.sum(back[:, :, :, :capacity], axis=1).astype(jnp.bfloat16)
    back_rows = back_rows.transpose(0, 2, 1, 3).reshape(slots, 2 * feat)
    slot_dots = jnp.sum(
        back[:, :, 0, capacity, :capacity] + back[:, :, 0, capacity, capacity:2 * capacity], axis=1
    ).reshape(slots)
    assign = picks.T.astype(jnp.bfloat16)
    a_both = jnp.dot(assign, back_rows, preferred_element_type=jnp.float32)
    a_out = a_both[:, :feat].reshape(tok_rows, top, feat)
    a_dx = a_both[:, feat:].reshape(tok_rows, top, feat)
    moe_out = jnp.sum(gates[:, :, None] * a_out, axis=1).astype(jnp.bfloat16)
    grad_tokens = jnp.sum(a_dx, axis=1).astype(jnp.bfloat16)
    assign_dots = jnp.sum(picks.T * slot_dots[None, :], axis=1).reshape(tok_rows, top)
    grad_gates = assign_dots / gates
    return (moe_out, grad_tokens, grad_gates)


def solution(mesh):
    return jax.shard_map(
        per_device,
        mesh=mesh,
        in_specs=(
            P("expert", ("pipe", "tensor")),
            P("expert", None),
            P("expert", None),
            P("expert", None, ("pipe", "tensor")),
            P("expert", None, ("pipe", "tensor")),
            P("expert", ("pipe", "tensor"), None),
            P("expert", ("pipe", "tensor")),
        ),
        out_specs=(
            P("expert", ("pipe", "tensor")),
            P("expert", ("pipe", "tensor")),
            P("expert", None),
        ),
        check_vma=False,
    )
```

```python
import jax
import jax.numpy as jnp
from jax import lax
from jax.sharding import PartitionSpec as P


def per_device(tokens, expert_ids, gates, w_gate, w_up, w_down, d_out):
    tok_rows = tokens.shape[0]
    feat = tokens.shape[1]
    top = expert_ids.shape[1]
    devices_all = lax.axis_size("expert")
    planes = lax.axis_size("pipe") * lax.axis_size("tensor")
    experts = min(8, devices_all)
    group = devices_all // experts
    capacity = min(
        tok_rows,
        max(2, max(5 * tok_rows * top // (4 * experts), (tok_rows * top + experts - 1) // experts)),
    )
    slots = experts * capacity
    rows_n = devices_all * capacity
    core = lax.axis_index("expert") % 2
    first_core = core == 0
    partner = [(i, i ^ 1) for i in range(devices_all)]
    flat_ids = expert_ids.reshape(-1)
    onehot = (flat_ids[:, None] == jnp.arange(experts, dtype=jnp.int32)[None, :]).astype(jnp.int32)
    position = jnp.sum(jnp.cumsum(onehot, axis=0) * onehot, axis=1) - 1
    slot_of = flat_ids * capacity + position
    picks = (jnp.arange(slots, dtype=jnp.int32)[:, None] == slot_of[None, :]).astype(jnp.float32)
    pick_rows = picks.reshape(slots, tok_rows, top)
    select_tok = jnp.sum(pick_rows, axis=2).astype(jnp.bfloat16)
    slot_gate = jnp.sum(pick_rows * gates[None, :, :], axis=(1, 2))
    both_in = jnp.concatenate([tokens, d_out], axis=1)
    chosen = jnp.dot(select_tok, both_in, preferred_element_type=jnp.float32)
    picked = chosen[:, :feat].astype(jnp.bfloat16)
    scaled = (chosen[:, feat:] * slot_gate[:, None]).astype(jnp.bfloat16)
    pair = jnp.stack(
        [picked.reshape(experts, capacity, feat), scaled.reshape(experts, capacity, feat)], axis=1
    )
    lanes = 128
    send = jnp.concatenate([pair] * (group // 2), axis=1).reshape(
        devices_all, capacity * feat // lanes, lanes
    )
    recv = lax.all_to_all(send, "expert", split_axis=0, concat_axis=0, tiled=True)
    recv = recv.reshape(rows_n, feat)
    spread = jnp.broadcast_to(recv[None], (planes,) + recv.shape)
    gathered = lax.all_to_all(spread, ("pipe", "tensor"), 0, 0, tiled=True)
    own_rows = gathered.transpose(1, 0, 2).reshape(rows_n, planes * feat)
    other_rows = lax.ppermute(own_rows, "expert", partner)
    rows_x = jnp.where(first_core, own_rows, other_rows)
    rows_dy = jnp.where(first_core, other_rows, own_rows)
    gate_proj = w_gate[0]
    up_proj = w_up[0]
    down_proj = w_down[0]
    contract_last = (((1,), (1,)), ((), ()))
    h_gate = jnp.dot(rows_x, gate_proj, preferred_element_type=jnp.float32)
    h_up = jnp.dot(rows_x, up_proj, preferred_element_type=jnp.float32)
    sig = jax.nn.sigmoid(h_gate)
    hidden = (h_gate * sig * h_up).astype(jnp.bfloat16)
    out_terms = jnp.dot(hidden, down_proj, preferred_element_type=jnp.float32).astype(jnp.bfloat16)
    d_hidden = lax.dot_general(
        rows_dy, down_proj, contract_last, preferred_element_type=jnp.float32
    )
    d_gate_h = (d_hidden * h_up * sig * (1.0 + h_gate * (1.0 - sig))).astype(jnp.bfloat16)
    d_up_h = (d_hidden * h_gate * sig).astype(jnp.bfloat16)
    dx_terms = lax.dot_general(
        d_gate_h, gate_proj, contract_last, preferred_element_type=jnp.float32
    )
    dx_terms = dx_terms + lax.dot_general(
        d_up_h, up_proj, contract_last, preferred_element_type=jnp.float32
    )
    dx_terms = dx_terms.astype(jnp.bfloat16)
    keep = jnp.where(first_core, out_terms, dx_terms)
    give = jnp.where(first_core, dx_terms, out_terms)
    got = lax.ppermute(give, "expert", partner)
    both_f32 = keep.astype(jnp.float32) + got.astype(jnp.float32)
    both = both_f32.astype(jnp.bfloat16)
    row_dots = jnp.sum(rows_dy.astype(jnp.float32) * both_f32, axis=1)
    dots_hi = row_dots.astype(jnp.bfloat16)
    dots_lo = (row_dots - dots_hi.astype(jnp.float32)).astype(jnp.bfloat16)
    dots_row = jnp.concatenate(
        [dots_hi, dots_lo, jnp.zeros((feat - 2 * rows_n,), jnp.bfloat16)]
    ).reshape(1, 1, feat)
    terms = both.reshape(rows_n, planes, feat).transpose(1, 0, 2)
    terms = jnp.concatenate([terms, jnp.broadcast_to(dots_row, (planes, 1, feat))], axis=1)
    reduced = lax.all_to_all(terms, ("pipe", "tensor"), 0, 0, tiled=True).astype(jnp.float32)
    shares = jnp.sum(reduced[:, :rows_n], axis=0).astype(jnp.bfloat16)
    dots_sum = jnp.sum(reduced[:, rows_n, :rows_n] + reduced[:, rows_n, rows_n:2 * rows_n], axis=0)
    back_hi = dots_sum.astype(jnp.bfloat16)
    back_lo = (dots_sum - back_hi.astype(jnp.float32)).astype(jnp.bfloat16)
    back_dots = jnp.concatenate(
        [
            back_hi.reshape(devices_all, capacity),
            back_lo.reshape(devices_all, capacity),
            jnp.zeros((devices_all, lanes - 2 * capacity), jnp.bfloat16),
        ],
        axis=1,
    )
    back_send = jnp.concatenate(
        [shares.reshape(devices_all, capacity * feat), back_dots], axis=1
    ).reshape(devices_all, capacity * feat // lanes + 1, lanes)
    back = lax.all_to_all(back_send, "expert", split_axis=0, concat_axis=0, tiled=True)
    back = back.reshape(devices_all, capacity * feat + lanes)
    back_part = back[:, : capacity * feat].astype(jnp.float32)
    back_part = back_part.reshape(experts, group // 2, 2, capacity, feat)
    back_tail = back[:, capacity * feat : capacity * feat + 2 * capacity].astype(jnp.float32)
    back_tail = back_tail.reshape(experts, group // 2, 2, 2 * capacity)
    back_rows = jnp.sum(back_part, axis=1).astype(jnp.bfloat16)
    back_rows = back_rows.transpose(0, 2, 1, 3).reshape(slots, 2 * feat)
    slot_dots = jnp.sum(
        back_tail[:, :, 0, :capacity] + back_tail[:, :, 0, capacity:], axis=1
    ).reshape(slots)
    assign = picks.T.astype(jnp.bfloat16)
    a_both = jnp.dot(assign, back_rows, preferred_element_type=jnp.float32)
    a_out = a_both[:, :feat].reshape(tok_rows, top, feat)
    a_dx = a_both[:, feat:].reshape(tok_rows, top, feat)
    moe_out = jnp.sum(gates[:, :, None] * a_out, axis=1).astype(jnp.bfloat16)
    grad_tokens = jnp.sum(a_dx, axis=1).astype(jnp.bfloat16)
    assign_dots = jnp.sum(picks.T * slot_dots[None, :], axis=1).reshape(tok_rows, top)
    grad_gates = assign_dots / gates
    return (moe_out, grad_tokens, grad_gates)


def solution(mesh):
    return jax.shard_map(
        per_device,
        mesh=mesh,
        in_specs=(
            P("expert", ("pipe", "tensor")),
            P("expert", None),
            P("expert", None),
            P("expert", None, ("pipe", "tensor")),
            P("expert", None, ("pipe", "tensor")),
            P("expert", ("pipe", "tensor"), None),
            P("expert", ("pipe", "tensor")),
        ),
        out_specs=(
            P("expert", ("pipe", "tensor")),
            P("expert", ("pipe", "tensor")),
            P("expert", None),
        ),
        check_vma=False,
    )
```
